128 devices in a mesh: ctx: 8 (over x, core), tp: 8 (over z_hi, y), dp: 2 (over z_lo).
Axes of the slice: x: 4, y: 4, z: 4 (z_hi: 2, z_lo: 2; z = z_hi * 2 + z_lo), core: 2. Of those that a mesh axis runs over, the one named last changes fastest.
Arguments:
- activations: bfloat16 [16384, 4096], P(('ctx', 'tp', 'dp')), may hold values from -6 to 6
- out_grad: bfloat16 [16384, 4096], P(('ctx', 'tp', 'dp')), may hold values from -6 to 6
- routes: int32 [16384, 8], P(('ctx', 'tp', 'dp')), may hold values from 0 to 127, all different within a row; in each aligned block of 128 rows (0 to 127, 128 to 255, ...) at most 12 rows name the same one
- gate_probs: bfloat16 [16384, 8], P(('ctx', 'tp', 'dp')), may hold values from 0.049804688 to 0.59765625
- saved_pre: bfloat16 [64, 2, 768, 1536], P(('ctx', 'tp'), 'dp'), may hold values from -6 to 6
- expert_weights: bfloat16 [64, 4096, 2304], P(('ctx', 'tp'), 'dp'), may hold values from -0.09375 to 0.09375
Outputs:
- input_grad: bfloat16 [16384, 4096], P(('ctx', 'tp', 'dp'))
- prob_grad: bfloat16 [16384, 8], P(('ctx', 'tp', 'dp'))
- weight_grad: bfloat16 [64, 4096, 2304], P(('ctx', 'tp'), 'dp')
The draws below stay inside these ranges and needn't reach their ends.
Inputs may be any that keep to these rules, and one draw needn't show every extreme that they name: `routes`: each row names 8 different experts. Within the rows of one device (aligned blocks of 128 rows) no expert is named more than 12 times, a bound that some block reaches.
All inputs are finite; a program needn't handle non-finite values.
Results may differ from the reference program's by a relative error of at most 0.02.
Values may be sent and summed in bfloat16 or wider, within the bound.
No kernel may reach another device: no remote copies, remote signals or barrier semaphores. Data moves between devices by JAX's collectives and lax.ppermute only.
A program may use at most 192 MiB of HBM per device.

```python
import math
import jax
import jax.numpy as jnp
import numpy as np
from jax import lax

D = 4096
H = 768
TOP = 8
T_DEV = 128
EXPERTS = 64
ROUTED = 128
CAP = 12
SLOTS = 768
TOKENS = 16384
N_DP = 2


def block_scale(own_key, extent, shards, smallest, high):
    loudness = 1.0
    for axis_at, shards_of in shards:
        draws = jax.random.uniform(jax.random.fold_in(jax.random.fold_in(own_key, 6), axis_at), (shards_of,), jnp.float32, smallest / len(shards), high / len(shards))
        loudness = loudness * jnp.repeat(jnp.exp(draws), extent[axis_at] // shards_of).reshape((-1,) + (1,) * (len(extent) - 1 - axis_at))
    return loudness


def assign_block(rng, own, number, rows, count, top, most, slope):
    ranking = jax.random.permutation(rng, count)
    heavy_load, usual = portions_of(count, rows * top, most, slope, True), portions_of(count, rows * top, most, slope, False)
    places = jnp.arange(count)

    def named(sizes, offset_by):
        used = int((sizes > 0).sum())
        fixed = max(1, used // 4)
        moved = fixed + (places - fixed + offset_by * (used - fixed)) % max(1, count - fixed)
        return jnp.zeros((count,), jnp.int32).at[ranking[jnp.where(places < fixed, places, moved)]].set(jnp.asarray(sizes, jnp.int32))

    sizes = jnp.where(number % 4 == 0, named(heavy_load, number // 4), named(usual, number - number // 4 - 1))
    mixed = jax.random.permutation(jax.random.fold_in(own, 3), count)
    giver, receiver = mixed[0:count // 2 * 2:2], mixed[1:count // 2 * 2:2]
    room = jnp.minimum(sizes[giver] - 1, most - sizes[receiver]) // 2
    room = jnp.where((giver == ranking[0]) | (receiver == ranking[0]) | (sizes[receiver] == 0), 0, jnp.maximum(room, 0))
    moved = jax.random.randint(jax.random.fold_in(own, 4), (count // 2,), 0, 1 << 20) % (room + 1)
    sizes = sizes.at[giver].add(-moved).at[receiver].add(moved)
    labels = jnp.searchsorted(jnp.cumsum(sizes), jnp.arange(rows * top), side="right").astype(jnp.int32)
    listing = labels.reshape(top, rows).T
    listing = listing[jax.random.permutation(jax.random.fold_in(own, 1), rows)]
    offset_by = jax.random.randint(jax.random.fold_in(own, 2), (rows, 1), 0, top)
    return jnp.take_along_axis(listing, (jnp.arange(top)[None, :] + offset_by) % top, axis=1)


def portions_of(number_of, total, bound, slope, full):
    loads = [(1 << 20) // math.isqrt(rank ** slope) + 1 for rank in range(1, number_of + 1)]
    largest = bound if full else min(bound, max(-(-total // number_of), total * loads[0] // sum(loads)))
    least = 1 if total - largest >= number_of - 1 else 0
    counts, spare = [largest] + [least] * (number_of - 1), total - largest - least * (number_of - 1)
    while spare > 0:
        movable = [i for i in range(1, number_of) if counts[i] < largest] or [i for i in range(1, number_of) if counts[i] < bound]
        mass, left = sum([loads[i] for i in movable]), spare
        for i in movable:
            extra = min(bound - counts[i], max(1, left * loads[i] // mass), spare)
            counts[i] = counts[i] + extra
            spare = spare - extra
    return np.array(counts)


def normal_values(key, extent, spread, bound, split=(), held_as=jnp.bfloat16):
    factor_of = block_scale(key, extent, split, -0.22, 0.18) if split else 1.0
    drawn = jax.random.normal(key, extent, jnp.float32) * spread * factor_of
    return jnp.minimum(jnp.maximum(drawn, -bound), bound).astype(held_as)


def setup_inputs(seed: int = 0) -> dict:
    streams_of = jax.random.split(jax.random.key(seed), 7)
    activations = normal_values(streams_of[0], (TOKENS, D), 1.0, 6.0, ((0, 128),))
    out_grad = normal_values(streams_of[1], (TOKENS, D), 1.0, 6.0, ((0, 128),))
    routes_keys = jax.random.split(jax.random.fold_in(streams_of[2], 1), TOKENS // T_DEV)
    routes_turns = jax.random.permutation(jax.random.fold_in(streams_of[2], 3), TOKENS // T_DEV)
    routes = jax.vmap(lambda own, number: assign_block(jax.random.fold_in(streams_of[2], 2), own, number, T_DEV, ROUTED, TOP, CAP, 1))(routes_keys, routes_turns).reshape((TOKENS, TOP))
    gate_probs = jnp.clip(0.049804688 + 0.54785156 * jax.random.uniform(streams_of[3], (TOKENS, TOP), jnp.float32) ** block_scale(streams_of[3], (TOKENS, TOP), ((0, 128),), -0.2, 0.2), 0.049804688, 0.59765625).astype(jnp.bfloat16)
    saved_pre = normal_values(streams_of[4], (EXPERTS, N_DP, SLOTS, 2 * H), 1.0, 6.0, ((0, 64), (1, 2)))
    expert_weights = normal_values(streams_of[5], (EXPERTS, D, 3 * H), D ** -0.5, 0.09375, ((0, 64), (1, 2)))
    return dict(activations=activations, out_grad=out_grad, routes=routes, gate_probs=gate_probs, saved_pre=saved_pre, expert_weights=expert_weights)


def slot_table(routes):
    blocks = TOKENS // T_DEV
    per_block = routes.reshape(blocks, T_DEV * TOP).astype(jnp.int32)
    in_window = per_block < EXPERTS
    onehot = (per_block[:, :, None] == jnp.arange(EXPERTS, dtype=jnp.int32)[None, None, :]).astype(jnp.int32)
    position = jnp.sum(jnp.cumsum(onehot, axis=1) * onehot, axis=2) - 1
    block_ids = jnp.arange(blocks, dtype=jnp.int32)[:, None]
    source = block_ids // N_DP
    replica = block_ids % N_DP
    slot_total = EXPERTS * N_DP * SLOTS
    flat_slot = (per_block * N_DP + replica) * SLOTS + source * CAP + position
    flat_slot = jnp.where(in_window, flat_slot, slot_total).astype(jnp.int32)
    route_ids = jnp.arange(TOKENS * TOP, dtype=jnp.int32)
    slot_routes = jnp.full((slot_total,), TOKENS * TOP, jnp.int32)
    slot_routes = slot_routes.at[flat_slot.reshape(-1)].set(route_ids, mode="drop")
    return slot_routes.reshape(EXPERTS, N_DP, SLOTS)


def expert_math(expert_rows, expert_grads, expert_probs, saved_rows, weights):
    pre_gate = saved_rows[:, :H].astype(jnp.float32)
    pre_up = saved_rows[:, H:].astype(jnp.float32)
    sigmoid_gate = jax.nn.sigmoid(pre_gate)
    activated = pre_gate * sigmoid_gate
    hidden_act = activated * pre_up
    down_grad = jnp.dot(expert_grads, weights[:, 2 * H:], preferred_element_type=jnp.float32)
    slot_prob = jnp.sum(hidden_act * down_grad, axis=1).astype(jnp.bfloat16)
    prob_column = expert_probs[:, None]
    scaled_grad = prob_column * down_grad
    gate_up_grad = jnp.concatenate(
        [scaled_grad * pre_up * sigmoid_gate * (1.0 + pre_gate * (1.0 - sigmoid_gate)), scaled_grad * activated],
        axis=1).astype(jnp.bfloat16)
    scaled_hidden = (prob_column * hidden_act).astype(jnp.bfloat16)
    row_grad = lax.dot_general(gate_up_grad, weights[:, :2 * H], (((1,), (1,)), ((), ())),
                               preferred_element_type=jnp.float32).astype(jnp.bfloat16)
    gate_up_term = lax.dot_general(expert_rows, gate_up_grad, (((0,), (0,)), ((), ())),
                                   preferred_element_type=jnp.float32)
    down_term = lax.dot_general(expert_grads, scaled_hidden, (((0,), (0,)), ((), ())),
                                preferred_element_type=jnp.float32)
    return slot_prob, row_grad, jnp.concatenate([gate_up_term, down_term], axis=1)


def reference(activations, out_grad, routes, gate_probs, saved_pre, expert_weights):
    slot_routes = slot_table(routes)
    route_total = TOKENS * TOP
    flat_probs = gate_probs.reshape(-1)

    def one_expert(accum, inputs):
        input_acc, prob_acc = accum
        expert_routes, saved_block, weights = inputs
        partial_value = jnp.zeros((D, 3 * H), jnp.float32)
        for replica in range(N_DP):
            routes_here = expert_routes[replica].astype(jnp.int32)
            filled = routes_here < route_total
            safe_ids = jnp.minimum(routes_here, route_total - 1).astype(jnp.int32)
            token_ids = (safe_ids // TOP).astype(jnp.int32)
            expert_rows = jnp.where(filled[:, None], activations[token_ids], jnp.zeros((), jnp.bfloat16))
            expert_grads = jnp.where(filled[:, None], out_grad[token_ids], jnp.zeros((), jnp.bfloat16))
            expert_probs = jnp.where(filled, flat_probs[safe_ids], jnp.zeros((), jnp.bfloat16)).astype(jnp.float32)
            slot_prob, row_grad, contrib = expert_math(expert_rows, expert_grads, expert_probs,
                                                       saved_block[replica], weights)
            rounded = lax.optimization_barrier(contrib.astype(jnp.bfloat16))
            partial_value = partial_value + rounded.astype(jnp.float32)
            target_tokens = jnp.where(filled, token_ids, TOKENS).astype(jnp.int32)
            input_acc = input_acc.at[target_tokens].add(row_grad.astype(jnp.float32), mode="drop")
            target_routes = jnp.where(filled, safe_ids, route_total).astype(jnp.int32)
            prob_acc = prob_acc.at[target_routes].set(slot_prob.astype(jnp.float32), mode="drop")
        return (input_acc, prob_acc), partial_value.astype(jnp.bfloat16)

    start = (jnp.zeros((TOKENS, D), jnp.float32), jnp.zeros((route_total,), jnp.float32))
    (input_acc, prob_acc), weight_grad = lax.scan(one_expert, start, (slot_routes, saved_pre, expert_weights))
    input_grad = input_acc.astype(jnp.bfloat16)
    prob_grad = prob_acc.reshape(TOKENS, TOP).astype(jnp.bfloat16)
    return (input_grad, prob_grad, weight_grad)
```

```python
import jax
import jax.numpy as jnp
from jax import lax
from jax.sharding import PartitionSpec as P

ALL = ("ctx", "tp", "dp")


def body(activations, out_grad, routes, gate_probs, saved_pre, expert_weights):
    tok_count = activations.shape[0]
    top_k = routes.shape[1]
    model_width = activations.shape[1]
    ctx_size = lax.axis_size("ctx")
    tp_size = lax.axis_size("tp")
    n_dp = lax.axis_size("dp")
    experts = ctx_size * tp_size
    slots_rep = saved_pre.shape[2]
    capacity = slots_rep // experts
    hidden = saved_pre.shape[3] // 2
    half = model_width // n_dp
    devices = experts * n_dp
    slots_all = n_dp * slots_rep
    lanes = 512
    rows_per_chunk = capacity * half // lanes
    f32 = jnp.float32
    bf16 = jnp.bfloat16

    flat_routes = routes.reshape(-1)
    route_count = flat_routes.shape[0]
    idx = jnp.arange(route_count, dtype=jnp.int32)
    same = (flat_routes[:, None] == flat_routes[None, :]) & (idx[None, :] < idx[:, None])
    position = jnp.sum(same.astype(jnp.int32), axis=1)
    in_window = flat_routes < experts
    slot_index = jnp.where(in_window, flat_routes * capacity + position, -1)
    slot_ids = jnp.arange(experts * capacity, dtype=jnp.int32)
    route_hit = slot_index[:, None] == slot_ids[None, :]
    token_hit = jnp.any(route_hit.reshape(tok_count, top_k, -1), axis=1)
    select = token_hit.astype(bf16).T.reshape(experts, capacity, tok_count)

    send_probs = jnp.sum(
        jnp.where(route_hit, gate_probs.reshape(-1)[:, None].astype(f32), 0.0), axis=0
    ).astype(bf16).reshape(experts, 1, capacity)
    send_probs = jnp.broadcast_to(send_probs, (experts, n_dp, capacity)).reshape(devices, capacity)

    def dispatch(x):
        x3 = x.reshape(tok_count, n_dp, half)
        sent = jnp.einsum("ept,thd->ehpd", select, x3, preferred_element_type=f32).astype(bf16)
        got = lax.all_to_all(
            sent.reshape(devices, rows_per_chunk, lanes), ALL, 0, 0, tiled=True
        )
        got = got.reshape(experts, n_dp, capacity, half).transpose(1, 0, 2, 3)
        return got.reshape(slots_all, half)

    recv_grads = dispatch(out_grad)
    recv_rows = dispatch(activations)
    got_probs = lax.all_to_all(send_probs, ALL, 0, 0, tiled=True)
    prob_column = (
        got_probs.reshape(experts, n_dp, capacity).transpose(1, 0, 2).reshape(slots_all, 1).astype(f32)
    )

    saved_rows = lax.all_gather(saved_pre[0, 0], "dp", axis=0, tiled=True)
    weights = expert_weights[0]
    down_part = weights[:, 2 * hidden :]
    gate_up_part = weights[:, : 2 * hidden]

    partial_down = jnp.dot(recv_grads, down_part, preferred_element_type=f32)
    other_down = lax.ppermute(partial_down, "dp", [(i, (i + 1) % n_dp) for i in range(n_dp)])
    down_grad = partial_down + other_down

    pre_gate = saved_rows[:, :hidden].astype(f32)
    pre_up = saved_rows[:, hidden:].astype(f32)
    sigmoid_gate = jax.nn.sigmoid(pre_gate)
    activated = pre_gate * sigmoid_gate
    hidden_act = activated * pre_up
    prob_slot = jnp.sum(hidden_act * down_grad, axis=1).astype(bf16)
    scaled_grad = prob_column * down_grad
    gate_up_grad = jnp.concatenate(
        [
            scaled_grad * pre_up * sigmoid_gate * (1.0 + pre_gate * (1.0 - sigmoid_gate)),
            scaled_grad * activated,
        ],
        axis=1,
    ).astype(bf16)
    scaled_hidden = (prob_column * hidden_act).astype(bf16)

    row_grad = lax.dot_general(
        gate_up_grad, gate_up_part, (((1,), (1,)), ((), ())), preferred_element_type=f32
    ).astype(bf16)
    gate_up_term = lax.dot_general(
        recv_rows, gate_up_grad, (((0,), (0,)), ((), ())), preferred_element_type=f32
    )
    down_term = lax.dot_general(
        recv_grads, scaled_hidden, (((0,), (0,)), ((), ())), preferred_element_type=f32
    )
    weight_grad = jnp.concatenate([gate_up_term, down_term], axis=1).astype(bf16)[None]

    ret = row_grad.reshape(n_dp, experts, capacity, half).transpose(1, 0, 2, 3)
    back = lax.all_to_all(ret.reshape(devices, rows_per_chunk, lanes), ALL, 0, 0, tiled=True)
    back = back.reshape(experts, n_dp, capacity, half)
    input_grad = jnp.einsum("ept,ehpd->thd", select, back, preferred_element_type=f32)
    input_grad = input_grad.reshape(tok_count, model_width).astype(bf16)

    ret_probs = prob_slot.reshape(n_dp, experts, capacity).transpose(1, 0, 2).reshape(devices, capacity)
    back_probs = lax.all_to_all(ret_probs, ALL, 0, 0, tiled=True)
    back_probs = back_probs.reshape(experts, n_dp, capacity)[:, 0].reshape(-1).astype(f32)
    prob_grad = jnp.sum(jnp.where(route_hit, back_probs[None, :], 0.0), axis=1)
    prob_grad = prob_grad.astype(bf16).reshape(tok_count, top_k)
    return (input_grad, prob_grad, weight_grad)


def solution(mesh):
    placed = (
        P(ALL, None),
        P(ALL, None),
        P(ALL, None),
        P(ALL, None),
        P(("ctx", "tp"), "dp", None, None),
        P(("ctx", "tp"), "dp", None),
    )
    return jax.shard_map(
        body,
        mesh=mesh,
        in_specs=placed,
        out_specs=(
            P(ALL, None),
            P(ALL, None),
            P(("ctx", "tp"), "dp", None),
        ),
        check_vma=False,
    )
```

```python
import jax
import jax.numpy as jnp
from jax import lax
from jax.sharding import PartitionSpec as P

ALL = ("ctx", "tp", "dp")
WIRE = ("dp", "ctx", "tp")


def body(activations, out_grad, routes, gate_probs, saved_pre, expert_weights):
    tok_count = activations.shape[0]
    top_k = routes.shape[1]
    model_width = activations.shape[1]
    ctx_size = lax.axis_size("ctx")
    tp_size = lax.axis_size("tp")
    n_dp = lax.axis_size("dp")
    experts = ctx_size * tp_size
    slots_rep = saved_pre.shape[2]
    capacity = slots_rep // experts
    cap = -(-capacity // 16) * 16
    hidden = saved_pre.shape[3] // 2
    half = model_width // n_dp
    devices = experts * n_dp
    slots_all = devices * cap
    f32 = jnp.float32
    bf16 = jnp.bfloat16

    flat_routes = routes.reshape(-1)
    route_count = flat_routes.shape[0]
    idx = jnp.arange(route_count, dtype=jnp.int32)
    same = (flat_routes[:, None] == flat_routes[None, :]) & (idx[None, :] < idx[:, None])
    position = jnp.sum(same.astype(jnp.int32), axis=1)
    in_window = flat_routes < experts
    slot_index = jnp.where(in_window, flat_routes * cap + position, -1)
    slot_ids = jnp.arange(experts * cap, dtype=jnp.int32)
    route_hit = slot_index[:, None] == slot_ids[None, :]
    token_hit = jnp.any(route_hit.reshape(tok_count, top_k, -1), axis=1)
    select = token_hit.astype(bf16).T

    send_probs = jnp.sum(
        jnp.where(route_hit, gate_probs.reshape(-1)[:, None].astype(f32), 0.0), axis=0
    ).astype(bf16)
    send_probs = jnp.broadcast_to(send_probs[None], (n_dp, experts * cap)).reshape(devices, cap)

    def dispatch(x):
        x3 = x.reshape(tok_count, n_dp, half)
        sent = jnp.einsum("st,thd->hsd", select, x3, preferred_element_type=f32).astype(bf16)
        got = lax.all_to_all(sent.reshape(devices, cap, half), WIRE, 0, 0, tiled=True)
        return got.reshape(slots_all, half)

    recv_grads = dispatch(out_grad)
    recv_rows = dispatch(activations)
    got_probs = lax.all_to_all(send_probs, WIRE, 0, 0, tiled=True)
    prob_column = got_probs.reshape(slots_all, 1).astype(f32)

    saved_rows = lax.all_gather(saved_pre[0, 0], "dp", axis=0, tiled=True)
    saved_rows = saved_rows.reshape(devices, capacity, 2 * hidden)
    saved_rows = jnp.pad(saved_rows, ((0, 0), (0, cap - capacity), (0, 0))).reshape(slots_all, -1)
    weights = expert_weights[0]
    down_part = weights[:, 2 * hidden :]
    gate_up_part = weights[:, : 2 * hidden]

    partial_down = jnp.dot(recv_grads, down_part, preferred_element_type=f32)
    used_down = partial_down.reshape(devices, cap, hidden)[:, :capacity].reshape(-1, hidden)
    other_down = lax.ppermute(used_down, "dp", [(i, (i + 1) % n_dp) for i in range(n_dp)])
    other_down = jnp.pad(
        other_down.reshape(devices, capacity, hidden), ((0, 0), (0, cap - capacity), (0, 0))
    ).reshape(slots_all, hidden)
    down_grad = partial_down + other_down

    pre_gate = saved_rows[:, :hidden].astype(f32)
    pre_up = saved_rows[:, hidden:].astype(f32)
    sigmoid_gate = jax.nn.sigmoid(pre_gate)
    activated = pre_gate * sigmoid_gate
    hidden_act = activated * pre_up
    prob_slot = jnp.sum(hidden_act * down_grad, axis=1).astype(bf16)
    scaled_grad = prob_column * down_grad
    gate_up_grad = jnp.concatenate(
        [
            scaled_grad * pre_up * sigmoid_gate * (1.0 + pre_gate * (1.0 - sigmoid_gate)),
            scaled_grad * activated,
        ],
        axis=1,
    ).astype(bf16)
    scaled_hidden = (prob_column * hidden_act).astype(bf16)

    row_grad = lax.dot_general(
        gate_up_grad, gate_up_part, (((1,), (1,)), ((), ())), preferred_element_type=f32
    ).astype(bf16)
    gate_up_term = lax.dot_general(
        recv_rows, gate_up_grad, (((0,), (0,)), ((), ())), preferred_element_type=f32
    )
    down_term = lax.dot_general(
        recv_grads, scaled_hidden, (((0,), (0,)), ((), ())), preferred_element_type=f32
    )
    weight_grad = jnp.concatenate([gate_up_term, down_term], axis=1).astype(bf16)[None]

    back = lax.all_to_all(row_grad.reshape(devices, cap, half), WIRE, 0, 0, tiled=True)
    back = back.reshape(n_dp, experts * cap, half)
    input_grad = lax.dot_general(
        select, back, (((0,), (1,)), ((), ())), preferred_element_type=f32
    )
    input_grad = input_grad.reshape(tok_count, model_width).astype(bf16)

    back_probs = lax.all_to_all(prob_slot.reshape(devices, cap), WIRE, 0, 0, tiled=True)
    back_probs = back_probs.reshape(n_dp, experts * cap)[0].astype(f32)
    prob_grad = jnp.sum(jnp.where(route_hit, back_probs[None, :], 0.0), axis=1)
    prob_grad = prob_grad.astype(bf16).reshape(tok_count, top_k)
    return (input_grad, prob_grad, weight_grad)


def solution(mesh):
    placed = (
        P(ALL, None),
        P(ALL, None),
        P(ALL, None),
        P(ALL, None),
        P(("ctx", "tp"), "dp", None, None),
        P(("ctx", "tp"), "dp", None),
    )
    return jax.shard_map(
        body,
        mesh=mesh,
        in_specs=placed,
        out_specs=(
            P(ALL, None),
            P(ALL, None),
            P(("ctx", "tp"), "dp", None),
        ),
        check_vma=False,
    )
```

```python
import jax
import jax.numpy as jnp
from jax import lax
from jax.sharding import PartitionSpec as P

ALL = ("ctx", "tp", "dp")
WIRE = ("dp", "ctx", "tp")


def body(activations, out_grad, routes, gate_probs, saved_pre, expert_weights):
    tok_count = activations.shape[0]
    top_k = routes.shape[1]
    model_width = activations.shape[1]
    ctx_size = lax.axis_size("ctx")
    tp_size = lax.axis_size("tp")
    n_dp = lax.axis_size("dp")
    experts = ctx_size * tp_size
    slots_rep = saved_pre.shape[2]
    capacity = slots_rep // experts
    cap = -(-capacity // 16) * 16
    hidden = saved_pre.shape[3] // 2
    half = model_width // n_dp
    devices = experts * n_dp
    slots_all = devices * cap
    f32 = jnp.float32
    bf16 = jnp.bfloat16

    flat_routes = routes.reshape(-1)
    route_count = flat_routes.shape[0]
    idx = jnp.arange(route_count, dtype=jnp.int32)
    same = (flat_routes[:, None] == flat_routes[None, :]) & (idx[None, :] < idx[:, None])
    position = jnp.sum(same.astype(jnp.int32), axis=1)
    in_window = flat_routes < experts
    slot_index = jnp.where(in_window, flat_routes * cap + position, -1)
    slot_ids = jnp.arange(experts * cap, dtype=jnp.int32)
    route_hit = slot_index[:, None] == slot_ids[None, :]
    token_hit = jnp.any(route_hit.reshape(tok_count, top_k, -1), axis=1)
    select = token_hit.astype(bf16).T

    send_probs = jnp.sum(
        jnp.where(route_hit, gate_probs.reshape(-1)[:, None].astype(f32), 0.0), axis=0
    ).astype(bf16)

    def dispatch(x):
        x3 = x.reshape(tok_count, n_dp, half)
        sent = jnp.einsum("st,thd->hsd", select, x3, preferred_element_type=f32).astype(bf16)
        got = lax.all_to_all(sent.reshape(devices, cap, half), WIRE, 0, 0, tiled=True)
        return got.reshape(slots_all, half)

    recv_grads = dispatch(out_grad)
    recv_rows = dispatch(activations)
    all_probs = lax.all_gather(send_probs.reshape(1, experts, cap), WIRE, axis=0, tiled=True)
    me = lax.axis_index("ctx") * tp_size + lax.axis_index("tp")
    got_probs = lax.dynamic_index_in_dim(all_probs, me, axis=1, keepdims=False)
    prob_column = got_probs.reshape(slots_all, 1).astype(f32)

    saved_rows = lax.all_gather(saved_pre[0, 0], "dp", axis=0, tiled=True)
    saved_rows = saved_rows.reshape(devices, capacity, 2 * hidden)
    saved_rows = jnp.pad(saved_rows, ((0, 0), (0, cap - capacity), (0, 0))).reshape(slots_all, -1)
    weights = expert_weights[0]
    down_part = weights[:, 2 * hidden :]
    gate_up_part = weights[:, : 2 * hidden]

    partial_down = jnp.dot(recv_grads, down_part, preferred_element_type=f32)
    used_down = partial_down.reshape(devices, cap, hidden)[:, :capacity].reshape(-1, hidden)
    other_down = lax.ppermute(used_down, "dp", [(i, (i + 1) % n_dp) for i in range(n_dp)])
    other_down = jnp.pad(
        other_down.reshape(devices, capacity, hidden), ((0, 0), (0, cap - capacity), (0, 0))
    ).reshape(slots_all, hidden)
    down_grad = partial_down + other_down

    pre_gate = saved_rows[:, :hidden].astype(f32)
    pre_up = saved_rows[:, hidden:].astype(f32)
    sigmoid_gate = jax.nn.sigmoid(pre_gate)
    activated = pre_gate * sigmoid_gate
    hidden_act = activated * pre_up
    prob_slot = jnp.sum(hidden_act * down_grad, axis=1).astype(bf16)
    scaled_grad = prob_column * down_grad
    gate_up_grad = jnp.concatenate(
        [
            scaled_grad * pre_up * sigmoid_gate * (1.0 + pre_gate * (1.0 - sigmoid_gate)),
            scaled_grad * activated,
        ],
        axis=1,
    ).astype(bf16)
    scaled_hidden = (prob_column * hidden_act).astype(bf16)

    row_grad = lax.dot_general(
        gate_up_grad, gate_up_part, (((1,), (1,)), ((), ())), preferred_element_type=f32
    ).astype(bf16)
    gate_up_term = lax.dot_general(
        recv_rows, gate_up_grad, (((0,), (0,)), ((), ())), preferred_element_type=f32
    )
    down_term = lax.dot_general(
        recv_grads, scaled_hidden, (((0,), (0,)), ((), ())), preferred_element_type=f32
    )
    weight_grad = jnp.concatenate([gate_up_term, down_term], axis=1).astype(bf16)[None]

    back = lax.all_to_all(row_grad.reshape(devices, cap, half), WIRE, 0, 0, tiled=True)
    back = back.reshape(n_dp, experts * cap, half)
    input_grad = lax.dot_general(
        select, back, (((0,), (1,)), ((), ())), preferred_element_type=f32
    )
    input_grad = input_grad.reshape(tok_count, model_width).astype(bf16)

    back_probs = lax.all_to_all(prob_slot.reshape(devices, cap), WIRE, 0, 0, tiled=True)
    back_probs = back_probs.reshape(n_dp, experts * cap)[0].astype(f32)
    prob_grad = jnp.sum(jnp.where(route_hit, back_probs[None, :], 0.0), axis=1)
    prob_grad = prob_grad.astype(bf16).reshape(tok_count, top_k)
    return (input_grad, prob_grad, weight_grad)


def solution(mesh):
    placed = (
        P(ALL, None),
        P(ALL, None),
        P(ALL, None),
        P(ALL, None),
        P(("ctx", "tp"), "dp", None, None),
        P(("ctx", "tp"), "dp", None),
    )
    return jax.shard_map(
        body,
        mesh=mesh,
        in_specs=placed,
        out_specs=(
            P(ALL, None),
            P(ALL, None),
            P(("ctx", "tp"), "dp", None),
        ),
        check_vma=False,
    )
```

```python
import jax
import jax.numpy as jnp
from jax import lax
from jax.sharding import PartitionSpec as P

ALL = ("ctx", "tp", "dp")


def body(activations, out_grad, routes, gate_probs, saved_pre, expert_weights):
    tok_count = activations.shape[0]
    top_k = routes.shape[1]
    model_width = activations.shape[1]
    ctx_size = lax.axis_size("ctx")
    tp_size = lax.axis_size("tp")
    n_dp = lax.axis_size("dp")
    experts = ctx_size * tp_size
    slots_rep = saved_pre.shape[2]
    capacity = slots_rep // experts
    hidden = saved_pre.shape[3] // 2
    half = model_width // n_dp
    devices = experts * n_dp
    slots_all = n_dp * slots_rep
    lanes = 512
    rows_per_chunk = capacity * half // lanes
    f32 = jnp.float32
    bf16 = jnp.bfloat16

    flat_routes = routes.reshape(-1)
    route_count = flat_routes.shape[0]
    idx = jnp.arange(route_count, dtype=jnp.int32)
    same = (flat_routes[:, None] == flat_routes[None, :]) & (idx[None, :] < idx[:, None])
    position = jnp.sum(same.astype(jnp.int32), axis=1)
    in_window = flat_routes < experts
    slot_index = jnp.where(in_window, flat_routes * capacity + position, -1)
    slot_ids = jnp.arange(experts * capacity, dtype=jnp.int32)
    route_hit = slot_index[:, None] == slot_ids[None, :]
    token_hit = jnp.any(route_hit.reshape(tok_count, top_k, -1), axis=1)
    select = token_hit.astype(bf16).T.reshape(experts, capacity, tok_count)
    flat_probs = gate_probs.reshape(-1).astype(f32)
    prob_select = jnp.sum(
        jnp.where(route_hit, flat_probs[:, None], 0.0).reshape(tok_count, top_k, -1), axis=1
    ).astype(bf16).T.reshape(experts, capacity, tok_count)

    def dispatch(x, sel):
        x3 = x.reshape(tok_count, n_dp, half)
        sent = jnp.einsum("ept,thd->ehpd", sel, x3, preferred_element_type=f32).astype(bf16)
        got = lax.all_to_all(
            sent.reshape(devices, rows_per_chunk, lanes), ALL, 0, 0, tiled=True
        )
        got = got.reshape(experts, n_dp, capacity, half).transpose(1, 0, 2, 3)
        return got.reshape(slots_all, half)

    recv_pgrads = dispatch(out_grad, prob_select)
    recv_rows = dispatch(activations, select)

    saved_rows = lax.all_gather(saved_pre[0, 0], "dp", axis=0, tiled=True)
    weights = expert_weights[0]
    down_part = weights[:, 2 * hidden :]
    gate_up_part = weights[:, : 2 * hidden]

    partial_down = jnp.dot(recv_pgrads, down_part, preferred_element_type=f32)
    other_down = lax.ppermute(
        partial_down.astype(bf16), "dp", [(i, (i + 1) % n_dp) for i in range(n_dp)]
    )
    scaled_grad = partial_down + other_down.astype(f32)

    pre_gate = saved_rows[:, :hidden].astype(f32)
    pre_up = saved_rows[:, hidden:].astype(f32)
    sigmoid_gate = jax.nn.sigmoid(pre_gate)
    activated = pre_gate * sigmoid_gate
    hidden_act = activated * pre_up
    scaled_slot_prob = jnp.sum(hidden_act * scaled_grad, axis=1)
    gate_up_grad = jnp.concatenate(
        [
            scaled_grad * pre_up * sigmoid_gate * (1.0 + pre_gate * (1.0 - sigmoid_gate)),
            scaled_grad * activated,
        ],
        axis=1,
    ).astype(bf16)

    row_grad = lax.dot_general(
        gate_up_grad, gate_up_part, (((1,), (1,)), ((), ())), preferred_element_type=f32
    ).astype(bf16)
    gate_up_term = lax.dot_general(
        recv_rows, gate_up_grad, (((0,), (0,)), ((), ())), preferred_element_type=f32
    )
    down_term = lax.dot_general(
        recv_pgrads, hidden_act.astype(bf16), (((0,), (0,)), ((), ())), preferred_element_type=f32
    )
    weight_grad = jnp.concatenate([gate_up_term, down_term], axis=1).astype(bf16)[None]

    ret = row_grad.reshape(n_dp, experts, capacity, half).transpose(1, 0, 2, 3)
    back = lax.all_to_all(ret.reshape(devices, rows_per_chunk, lanes), ALL, 0, 0, tiled=True)
    back = back.reshape(experts, n_dp, capacity, half)
    input_grad = jnp.einsum("ept,ehpd->thd", select, back, preferred_element_type=f32)
    input_grad = input_grad.reshape(tok_count, model_width).astype(bf16)

    ret_probs = scaled_slot_prob.reshape(n_dp, experts, capacity).transpose(1, 0, 2)
    back_probs = lax.all_to_all(ret_probs.reshape(devices, capacity), ALL, 0, 0, tiled=True)
    back_probs = back_probs.reshape(experts, n_dp, capacity)[:, 0].reshape(-1)
    picked = jnp.sum(jnp.where(route_hit, back_probs[None, :], 0.0), axis=1)
    prob_grad = jnp.where(in_window, picked / flat_probs, 0.0)
    prob_grad = prob_grad.astype(bf16).reshape(tok_count, top_k)
    return (input_grad, prob_grad, weight_grad)


def solution(mesh):
    placed = (
        P(ALL, None),
        P(ALL, None),
        P(ALL, None),
        P(ALL, None),
        P(("ctx", "tp"), "dp", None, None),
        P(("ctx", "tp"), "dp", None),
    )
    return jax.shard_map(
        body,
        mesh=mesh,
        in_specs=placed,
        out_specs=(
            P(ALL, None),
            P(ALL, None),
            P(("ctx", "tp"), "dp", None),
        ),
        check_vma=False,
    )
```

```python
import jax
import jax.numpy as jnp
from jax import lax
from jax.sharding import PartitionSpec as P

ALL = ("ctx", "tp", "dp")
WIRE = ("dp", "ctx", "tp")


def body(activations, out_grad, routes, gate_probs, saved_pre, expert_weights):
    tok_count = activations.shape[0]
    top_k = routes.shape[1]
    model_width = activations.shape[1]
    ctx_size = lax.axis_size("ctx")
    tp_size = lax.axis_size("tp")
    n_dp = lax.axis_size("dp")
    experts = ctx_size * tp_size
    slots_rep = saved_pre.shape[2]
    capacity = slots_rep // experts
    hidden = saved_pre.shape[3] // 2
    half = model_width // n_dp
    devices = experts * n_dp
    slots_all = n_dp * slots_rep
    lanes = 512
    rows_per_chunk = capacity * half // lanes
    f32 = jnp.float32
    bf16 = jnp.bfloat16

    flat_routes = routes.reshape(-1)
    route_count = flat_routes.shape[0]
    idx = jnp.arange(route_count, dtype=jnp.int32)
    same = (flat_routes[:, None] == flat_routes[None, :]) & (idx[None, :] < idx[:, None])
    position = jnp.sum(same.astype(jnp.int32), axis=1)
    in_window = flat_routes < experts
    slot_index = jnp.where(in_window, flat_routes * capacity + position, -1)
    slot_ids = jnp.arange(experts * capacity, dtype=jnp.int32)
    route_hit = slot_index[:, None] == slot_ids[None, :]
    token_hit = jnp.any(route_hit.reshape(tok_count, top_k, -1), axis=1)
    select = token_hit.astype(bf16).T
    flat_probs = gate_probs.reshape(-1).astype(f32)
    prob_select = jnp.sum(
        jnp.where(route_hit, flat_probs[:, None], 0.0).reshape(tok_count, top_k, -1), axis=1
    ).astype(bf16).T

    def dispatch(x, sel):
        x3 = x.reshape(tok_count, n_dp, half)
        sent = jnp.einsum("st,thd->hsd", sel, x3, preferred_element_type=f32).astype(bf16)
        got = lax.all_to_all(
            sent.reshape(devices, rows_per_chunk, lanes), WIRE, 0, 0, tiled=True
        )
        return got.reshape(slots_all, half)

    recv_pgrads = dispatch(out_grad, prob_select)
    recv_rows = dispatch(activations, select)

    own_saved = saved_pre[0, 0]
    if n_dp == 2:
        other_saved = lax.ppermute(own_saved, "dp", [(0, 1), (1, 0)])
        first = lax.axis_index("dp") == 0
        saved_rows = jnp.where(
            first,
            jnp.concatenate([own_saved, other_saved], axis=0),
            jnp.concatenate([other_saved, own_saved], axis=0),
        )
    else:
        saved_rows = lax.all_gather(own_saved, "dp", axis=0, tiled=True)
    weights = expert_weights[0]
    down_part = weights[:, 2 * hidden :]
    gate_up_part = weights[:, : 2 * hidden]

    partial_down = jnp.dot(recv_pgrads, down_part, preferred_element_type=f32)
    other_down = lax.ppermute(
        partial_down.astype(bf16), "dp", [(i, (i + 1) % n_dp) for i in range(n_dp)]
    )
    scaled_grad = partial_down + other_down.astype(f32)

    pre_gate = saved_rows[:, :hidden].astype(f32)
    pre_up = saved_rows[:, hidden:].astype(f32)
    sigmoid_gate = jax.nn.sigmoid(pre_gate)
    activated = pre_gate * sigmoid_gate
    hidden_act = activated * pre_up
    scaled_slot_prob = jnp.sum(hidden_act * scaled_grad, axis=1)
    gate_up_grad = jnp.concatenate(
        [
            scaled_grad * pre_up * sigmoid_gate * (1.0 + pre_gate * (1.0 - sigmoid_gate)),
            scaled_grad * activated,
        ],
        axis=1,
    ).astype(bf16)

    row_grad = lax.dot_general(
        gate_up_grad, gate_up_part, (((1,), (1,)), ((), ())), preferred_element_type=f32
    ).astype(bf16)
    gate_up_term = lax.dot_general(
        recv_rows, gate_up_grad, (((0,), (0,)), ((), ())), preferred_element_type=f32
    )
    down_term = lax.dot_general(
        recv_pgrads, hidden_act.astype(bf16), (((0,), (0,)), ((), ())), preferred_element_type=f32
    )
    weight_grad = jnp.concatenate([gate_up_term, down_term], axis=1).astype(bf16)[None]

    back = lax.all_to_all(row_grad.reshape(devices, rows_per_chunk, lanes), WIRE, 0, 0, tiled=True)
    back = back.reshape(n_dp, experts * capacity, half)
    input_grad = jnp.einsum("st,hsd->thd", select, back, preferred_element_type=f32)
    input_grad = input_grad.reshape(tok_count, model_width).astype(bf16)

    back_probs = lax.all_to_all(scaled_slot_prob.reshape(devices, capacity), WIRE, 0, 0, tiled=True)
    back_probs = back_probs.reshape(n_dp, experts * capacity)[0]
    picked = jnp.sum(jnp.where(route_hit, back_probs[None, :], 0.0), axis=1)
    prob_grad = jnp.where(in_window, picked / flat_probs, 0.0)
    prob_grad = prob_grad.astype(bf16).reshape(tok_count, top_k)
    return (input_grad, prob_grad, weight_grad)


def solution(mesh):
    placed = (
        P(ALL, None),
        P(ALL, None),
        P(ALL, None),
        P(ALL, None),
        P(("ctx", "tp"), "dp", None, None),
        P(("ctx", "tp"), "dp", None),
    )
    return jax.shard_map(
        body,
        mesh=mesh,
        in_specs=placed,
        out_specs=(
            P(ALL, None),
            P(ALL, None),
            P(("ctx", "tp"), "dp", None),
        ),
        check_vma=False,
    )
```

```python
import jax
import jax.numpy as jnp
from jax import lax
from jax.sharding import PartitionSpec as P

ALL = ("ctx", "tp", "dp")
WIRE = ("dp", "ctx", "tp")


def body(activations, out_grad, routes, gate_probs, saved_pre, expert_weights):
    tok_count = activations.shape[0]
    top_k = routes.shape[1]
    model_width = activations.shape[1]
    ctx_size = lax.axis_size("ctx")
    tp_size = lax.axis_size("tp")
    n_dp = lax.axis_size("dp")
    experts = ctx_size * tp_size
    slots_rep = saved_pre.shape[2]
    capacity = slots_rep // experts
    hidden = saved_pre.shape[3] // 2
    half = model_width // n_dp
    devices = experts * n_dp
    slots_all = n_dp * slots_rep
    lanes = 512
    rows_per_chunk = capacity * half // lanes
    f32 = jnp.float32
    bf16 = jnp.bfloat16

    flat_routes = routes.reshape(-1)
    route_count = flat_routes.shape[0]
    idx = jnp.arange(route_count, dtype=jnp.int32)
    same = (flat_routes[:, None] == flat_routes[None, :]) & (idx[None, :] < idx[:, None])
    position = jnp.sum(same.astype(jnp.int32), axis=1)
    in_window = flat_routes < experts
    slot_index = jnp.where(in_window, flat_routes * capacity + position, -1)
    slot_ids = jnp.arange(experts * capacity, dtype=jnp.int32)
    route_hit = slot_index[:, None] == slot_ids[None, :]
    flat_probs = gate_probs.reshape(-1).astype(f32)

    blocks = half // lanes
    wide_rows = experts * capacity * blocks
    wide_slot = jnp.where(in_window, slot_index * blocks, -blocks).reshape(tok_count, 1, top_k)
    wide_target = wide_slot + jnp.arange(blocks, dtype=jnp.int32).reshape(1, blocks, 1)
    wide_ids = jnp.arange(wide_rows, dtype=jnp.int32)
    wide_hit = wide_target.reshape(1, tok_count * blocks, top_k) == wide_ids.reshape(-1, 1, 1)
    wide_select = jnp.any(wide_hit, axis=2).astype(bf16)
    wide_probs = jnp.broadcast_to(
        gate_probs.reshape(tok_count, 1, top_k), (tok_count, blocks, top_k)
    ).reshape(1, tok_count * blocks, top_k)
    wide_prob_select = jnp.sum(jnp.where(wide_hit, wide_probs, 0.0), axis=2).astype(bf16)
    gather_hit = wide_target.transpose(1, 0, 2)[:, :, None, :] == wide_ids.reshape(1, 1, -1, 1)
    gather_back = jnp.any(gather_hit, axis=3).astype(bf16)

    def dispatch(x, sel):
        xb = x.reshape(tok_count, n_dp, blocks, lanes).transpose(1, 0, 2, 3)
        xb = xb.reshape(n_dp, tok_count * blocks, lanes)
        sent = jnp.einsum("qk,hkl->hql", sel, xb, preferred_element_type=f32).astype(bf16)
        got = lax.all_to_all(
            sent.reshape(devices, rows_per_chunk, lanes), WIRE, 0, 0, tiled=True
        )
        return got.reshape(slots_all, half)

    recv_pgrads = dispatch(out_grad, wide_prob_select)
    recv_rows = dispatch(activations, wide_select)

    own_saved = saved_pre[0, 0]
    if n_dp == 2:
        other_saved = lax.ppermute(own_saved, "dp", [(0, 1), (1, 0)])
        first = lax.axis_index("dp") == 0
        saved_rows = jnp.where(
            first,
            jnp.concatenate([own_saved, other_saved], axis=0),
            jnp.concatenate([other_saved, own_saved], axis=0),
        )
    else:
        saved_rows = lax.all_gather(own_saved, "dp", axis=0, tiled=True)
    weights = expert_weights[0]
    down_part = weights[:, 2 * hidden :]
    gate_up_part = weights[:, : 2 * hidden]

    partial_down = jnp.dot(recv_pgrads, down_part, preferred_element_type=f32)
    other_down = lax.ppermute(
        partial_down.astype(bf16), "dp", [(i, (i + 1) % n_dp) for i in range(n_dp)]
    )
    scaled_grad = partial_down + other_down.astype(f32)

    pre_gate = saved_rows[:, :hidden].astype(f32)
    pre_up = saved_rows[:, hidden:].astype(f32)
    sigmoid_gate = jax.nn.sigmoid(pre_gate)
    activated = pre_gate * sigmoid_gate
    hidden_act = activated * pre_up
    scaled_slot_prob = jnp.sum(hidden_act * scaled_grad, axis=1)
    gate_up_grad = jnp.concatenate(
        [
            scaled_grad * pre_up * sigmoid_gate * (1.0 + pre_gate * (1.0 - sigmoid_gate)),
            scaled_grad * activated,
        ],
        axis=1,
    ).astype(bf16)

    row_grad = lax.dot_general(
        gate_up_grad, gate_up_part, (((1,), (1,)), ((), ())), preferred_element_type=f32
    ).astype(bf16)
    gate_up_term = lax.dot_general(
        recv_rows, gate_up_grad, (((0,), (0,)), ((), ())), preferred_element_type=f32
    )
    down_term = lax.dot_general(
        recv_pgrads, hidden_act.astype(bf16), (((0,), (0,)), ((), ())), preferred_element_type=f32
    )
    weight_grad = jnp.concatenate([gate_up_term, down_term], axis=1).astype(bf16)[None]

    back = lax.all_to_all(row_grad.reshape(devices, rows_per_chunk, lanes), WIRE, 0, 0, tiled=True)
    back = back.reshape(n_dp, -1, lanes)
    input_grad = jnp.einsum("ctk,hkl->thcl", gather_back, back, preferred_element_type=f32)
    input_grad = input_grad.reshape(tok_count, model_width).astype(bf16)

    back_probs = lax.all_to_all(scaled_slot_prob.reshape(devices, capacity), WIRE, 0, 0, tiled=True)
    back_probs = back_probs.reshape(n_dp, experts * capacity)[0]
    picked = jnp.sum(jnp.where(route_hit, back_probs[None, :], 0.0), axis=1)
    prob_grad = jnp.where(in_window, picked / flat_probs, 0.0)
    prob_grad = prob_grad.astype(bf16).reshape(tok_count, top_k)
    return (input_grad, prob_grad, weight_grad)


def solution(mesh):
    placed = (
        P(ALL, None),
        P(ALL, None),
        P(ALL, None),
        P(ALL, None),
        P(("ctx", "tp"), "dp", None, None),
        P(("ctx", "tp"), "dp", None),
    )
    return jax.shard_map(
        body,
        mesh=mesh,
        in_specs=placed,
        out_specs=(
            P(ALL, None),
            P(ALL, None),
            P(("ctx", "tp"), "dp", None),
        ),
        check_vma=False,
    )
```

```python
import jax
import jax.numpy as jnp
from jax import lax
from jax.sharding import PartitionSpec as P

ALL = ("ctx", "tp", "dp")
WIRE = ("dp", "ctx", "tp")


def body(activations, out_grad, routes, gate_probs, saved_pre, expert_weights):
    tok_count = activations.shape[0]
    top_k = routes.shape[1]
    model_width = activations.shape[1]
    ctx_size = lax.axis_size("ctx")
    tp_size = lax.axis_size("tp")
    n_dp = lax.axis_size("dp")
    experts = ctx_size * tp_size
    slots_rep = saved_pre.shape[2]
    capacity = slots_rep // experts
    hidden = saved_pre.shape[3] // 2
    half = model_width // n_dp
    devices = experts * n_dp
    slots_all = n_dp * slots_rep
    lanes = 512
    rows_per_chunk = capacity * half // lanes
    f32 = jnp.float32
    bf16 = jnp.bfloat16

    flat_routes = routes.reshape(-1)
    route_count = flat_routes.shape[0]
    idx = jnp.arange(route_count, dtype=jnp.int32)
    same = (flat_routes[:, None] == flat_routes[None, :]) & (idx[None, :] < idx[:, None])
    position = jnp.sum(same.astype(jnp.int32), axis=1)
    in_window = flat_routes < experts
    slot_index = jnp.where(in_window, flat_routes * capacity + position, -1)
    slot_ids = jnp.arange(experts * capacity, dtype=jnp.int32)
    route_hit = slot_index[:, None] == slot_ids[None, :]
    flat_probs = gate_probs.reshape(-1).astype(f32)

    blocks = half // lanes
    wide_rows = experts * capacity * blocks
    route_token = (idx // top_k).reshape(-1, 1)
    slot_filled = jnp.any(route_hit, axis=0)
    slot_token = jnp.where(slot_filled, jnp.sum(jnp.where(route_hit, route_token, 0), axis=0), -1)
    slot_prob = jnp.sum(jnp.where(route_hit, flat_probs[:, None], 0.0), axis=0)
    block_ids = jnp.arange(blocks, dtype=jnp.int32)
    row_key = (slot_token[:, None] * blocks + block_ids[None, :]).reshape(wide_rows)
    row_prob = jnp.broadcast_to(slot_prob[:, None], (experts * capacity, blocks)).reshape(wide_rows)
    col_ids = jnp.arange(tok_count * blocks, dtype=jnp.int32)
    wide_hit = row_key[:, None] == col_ids[None, :]
    wide_select = wide_hit.astype(bf16)
    wide_prob_select = jnp.where(wide_hit, row_prob[:, None], 0.0).astype(bf16)
    gather_key = col_ids.reshape(tok_count, blocks).T.reshape(blocks, tok_count, 1)
    gather_back = (gather_key == row_key.reshape(1, 1, -1)).astype(bf16)

    def dispatch(x, sel):
        xb = x.reshape(tok_count, n_dp, blocks, lanes).transpose(1, 0, 2, 3)
        xb = xb.reshape(n_dp, tok_count * blocks, lanes)
        sent = jnp.einsum("qk,hkl->hql", sel, xb, preferred_element_type=f32).astype(bf16)
        got = lax.all_to_all(
            sent.reshape(devices, rows_per_chunk, lanes), WIRE, 0, 0, tiled=True
        )
        return got.reshape(slots_all, half)

    recv_pgrads = dispatch(out_grad, wide_prob_select)
    recv_rows = dispatch(activations, wide_select)

    own_saved = saved_pre[0, 0]
    if n_dp == 2:
        other_saved = lax.ppermute(own_saved, "dp", [(0, 1), (1, 0)])
        first = lax.axis_index("dp") == 0
        saved_rows = jnp.where(
            first,
            jnp.concatenate([own_saved, other_saved], axis=0),
            jnp.concatenate([other_saved, own_saved], axis=0),
        )
    else:
        saved_rows = lax.all_gather(own_saved, "dp", axis=0, tiled=True)
    weights = expert_weights[0]
    down_part = weights[:, 2 * hidden :]
    gate_up_part = weights[:, : 2 * hidden]

    partial_down = jnp.dot(recv_pgrads, down_part, preferred_element_type=f32)
    other_down = lax.ppermute(
        partial_down.astype(bf16), "dp", [(i, (i + 1) % n_dp) for i in range(n_dp)]
    )
    scaled_grad = partial_down + other_down.astype(f32)

    pre_gate = saved_rows[:, :hidden].astype(f32)
    pre_up = saved_rows[:, hidden:].astype(f32)
    sigmoid_gate = jax.nn.sigmoid(pre_gate)
    activated = pre_gate * sigmoid_gate
    hidden_act = activated * pre_up
    scaled_slot_prob = jnp.sum(hidden_act * scaled_grad, axis=1)
    gate_up_grad = jnp.concatenate(
        [
            scaled_grad * pre_up * sigmoid_gate * (1.0 + pre_gate * (1.0 - sigmoid_gate)),
            scaled_grad * activated,
        ],
        axis=1,
    ).astype(bf16)

    row_grad = lax.dot_general(
        gate_up_grad, gate_up_part, (((1,), (1,)), ((), ())), preferred_element_type=f32
    ).astype(bf16)
    gate_up_term = lax.dot_general(
        recv_rows, gate_up_grad, (((0,), (0,)), ((), ())), preferred_element_type=f32
    )
    down_term = lax.dot_general(
        recv_pgrads, hidden_act.astype(bf16), (((0,), (0,)), ((), ())), preferred_element_type=f32
    )
    weight_grad = jnp.concatenate([gate_up_term, down_term], axis=1).astype(bf16)[None]

    back = lax.all_to_all(row_grad.reshape(devices, rows_per_chunk, lanes), WIRE, 0, 0, tiled=True)
    back = back.reshape(n_dp, -1, lanes)
    input_grad = jnp.einsum("ctk,hkl->thcl", gather_back, back, preferred_element_type=f32)
    input_grad = input_grad.reshape(tok_count, model_width).astype(bf16)

    back_probs = lax.all_to_all(scaled_slot_prob.reshape(devices, capacity), WIRE, 0, 0, tiled=True)
    back_probs = back_probs.reshape(n_dp, experts * capacity)[0]
    picked = jnp.sum(jnp.where(route_hit, back_probs[None, :], 0.0), axis=1)
    prob_grad = jnp.where(in_window, picked / flat_probs, 0.0)
    prob_grad = prob_grad.astype(bf16).reshape(tok_count, top_k)
    return (input_grad, prob_grad, weight_grad)


def solution(mesh):
    placed = (
        P(ALL, None),
        P(ALL, None),
        P(ALL, None),
        P(ALL, None),
        P(("ctx", "tp"), "dp", None, None),
        P(("ctx", "tp"), "dp", None),
    )
    return jax.shard_map(
        body,
        mesh=mesh,
        in_specs=placed,
        out_specs=(
            P(ALL, None),
            P(ALL, None),
            P(("ctx", "tp"), "dp", None),
        ),
        check_vma=False,
    )
```

```python
import jax
import jax.numpy as jnp
from jax import lax
from jax.sharding import PartitionSpec as P

ALL = ("ctx", "tp", "dp")
WIRE = ("dp", "ctx", "tp")


def body(activations, out_grad, routes, gate_probs, saved_pre, expert_weights):
    tok_count = activations.shape[0]
    top_k = routes.shape[1]
    model_width = activations.shape[1]
    ctx_size = lax.axis_size("ctx")
    tp_size = lax.axis_size("tp")
    n_dp = lax.axis_size("dp")
    experts = ctx_size * tp_size
    slots_rep = saved_pre.shape[2]
    capacity = slots_rep // experts
    hidden = saved_pre.shape[3] // 2
    half = model_width // n_dp
    devices = experts * n_dp
    slots_all = n_dp * slots_rep
    lanes = 512
    rows_per_chunk = capacity * half // lanes
    f32 = jnp.float32
    bf16 = jnp.bfloat16

    flat_routes = routes.reshape(-1)
    route_count = flat_routes.shape[0]
    idx = jnp.arange(route_count, dtype=jnp.int32)
    same = (flat_routes[:, None] == flat_routes[None, :]) & (idx[None, :] < idx[:, None])
    position = jnp.sum(same.astype(jnp.int32), axis=1)
    in_window = flat_routes < experts
    slot_index = jnp.where(in_window, flat_routes * capacity + position, -1)
    slot_ids = jnp.arange(experts * capacity, dtype=jnp.int32)
    route_hit = slot_index[:, None] == slot_ids[None, :]
    flat_probs = gate_probs.reshape(-1).astype(f32)

    blocks = half // lanes
    wide_rows = experts * capacity * blocks
    route_token = (idx // top_k).reshape(-1, 1)
    slot_filled = jnp.any(route_hit, axis=0)
    slot_token = jnp.where(slot_filled, jnp.sum(jnp.where(route_hit, route_token, 0), axis=0), -1)
    slot_prob = jnp.sum(jnp.where(route_hit, flat_probs[:, None], 0.0), axis=0)
    block_ids = jnp.arange(blocks, dtype=jnp.int32)
    row_key = jnp.where(
        slot_filled[:, None], block_ids[None, :] * tok_count + slot_token[:, None], -1
    ).reshape(wide_rows)
    row_prob = jnp.broadcast_to(slot_prob[:, None], (experts * capacity, blocks)).reshape(wide_rows)
    col_ids = jnp.arange(tok_count * blocks, dtype=jnp.int32)
    wide_hit = row_key[:, None] == col_ids[None, :]
    wide_select = wide_hit.astype(bf16)
    wide_prob_select = jnp.where(wide_hit, row_prob[:, None], 0.0).astype(bf16)
    gather_key = col_ids.reshape(blocks, tok_count, 1)
    gather_back = (gather_key == row_key.reshape(1, 1, -1)).astype(bf16)

    def dispatch(x, sel):
        xb = x.reshape(tok_count, n_dp * blocks, lanes).transpose(1, 0, 2)
        xb = xb.reshape(n_dp, blocks * tok_count, lanes)
        sent = jnp.einsum("qk,hkl->hql", sel, xb, preferred_element_type=f32).astype(bf16)
        got = lax.all_to_all(
            sent.reshape(devices, rows_per_chunk, lanes), WIRE, 0, 0, tiled=True
        )
        return got.reshape(slots_all, half)

    recv_pgrads = dispatch(out_grad, wide_prob_select)
    recv_rows = dispatch(activations, wide_select)

    own_saved = saved_pre[0, 0]
    if n_dp == 2:
        other_saved = lax.ppermute(own_saved, "dp", [(0, 1), (1, 0)])
        first = lax.axis_index("dp") == 0
        saved_rows = jnp.where(
            first,
            jnp.concatenate([own_saved, other_saved], axis=0),
            jnp.concatenate([other_saved, own_saved], axis=0),
        )
    else:
        saved_rows = lax.all_gather(own_saved, "dp", axis=0, tiled=True)
    weights = expert_weights[0]
    down_part = weights[:, 2 * hidden :]
    gate_up_part = weights[:, : 2 * hidden]

    partial_down = jnp.dot(recv_pgrads, down_part, preferred_element_type=f32)
    other_down = lax.ppermute(
        partial_down.astype(bf16), "dp", [(i, (i + 1) % n_dp) for i in range(n_dp)]
    )
    scaled_grad = partial_down + other_down.astype(f32)

    pre_gate = saved_rows[:, :hidden].astype(f32)
    pre_up = saved_rows[:, hidden:].astype(f32)
    sigmoid_gate = jax.nn.sigmoid(pre_gate)
    activated = pre_gate * sigmoid_gate
    hidden_act = activated * pre_up
    scaled_slot_prob = jnp.sum(hidden_act * scaled_grad, axis=1)
    gate_up_grad = jnp.concatenate(
        [
            scaled_grad * pre_up * sigmoid_gate * (1.0 + pre_gate * (1.0 - sigmoid_gate)),
            scaled_grad * activated,
        ],
        axis=1,
    ).astype(bf16)

    row_grad = lax.dot_general(
        gate_up_grad, gate_up_part, (((1,), (1,)), ((), ())), preferred_element_type=f32
    ).astype(bf16)
    gate_up_term = lax.dot_general(
        recv_rows, gate_up_grad, (((0,), (0,)), ((), ())), preferred_element_type=f32
    )
    down_term = lax.dot_general(
        recv_pgrads, hidden_act.astype(bf16), (((0,), (0,)), ((), ())), preferred_element_type=f32
    )
    weight_grad = jnp.concatenate([gate_up_term, down_term], axis=1).astype(bf16)[None]

    back = lax.all_to_all(row_grad.reshape(devices, rows_per_chunk, lanes), WIRE, 0, 0, tiled=True)
    back = back.reshape(n_dp, -1, lanes)
    input_grad = jnp.einsum("ctk,hkl->thcl", gather_back, back, preferred_element_type=f32)
    input_grad = input_grad.reshape(tok_count, model_width).astype(bf16)

    back_probs = lax.all_to_all(scaled_slot_prob.reshape(devices, capacity), WIRE, 0, 0, tiled=True)
    back_probs = back_probs.reshape(n_dp, experts * capacity)[0]
    picked = jnp.sum(jnp.where(route_hit, back_probs[None, :], 0.0), axis=1)
    prob_grad = jnp.where(in_window, picked / flat_probs, 0.0)
    prob_grad = prob_grad.astype(bf16).reshape(tok_count, top_k)
    return (input_grad, prob_grad, weight_grad)


def solution(mesh):
    placed = (
        P(ALL, None),
        P(ALL, None),
        P(ALL, None),
        P(ALL, None),
        P(("ctx", "tp"), "dp", None, None),
        P(("ctx", "tp"), "dp", None),
    )
    return jax.shard_map(
        body,
        mesh=mesh,
        in_specs=placed,
        out_specs=(
            P(ALL, None),
            P(ALL, None),
            P(("ctx", "tp"), "dp", None),
        ),
        check_vma=False,
    )
```

```python
import jax
import jax.numpy as jnp
from jax import lax
from jax.sharding import PartitionSpec as P

ALL = ("ctx", "tp", "dp")
WIRE = ("dp", "ctx", "tp")


def body(activations, out_grad, routes, gate_probs, saved_pre, expert_weights):
    tok_count = activations.shape[0]
    top_k = routes.shape[1]
    model_width = activations.shape[1]
    ctx_size = lax.axis_size("ctx")
    tp_size = lax.axis_size("tp")
    n_dp = lax.axis_size("dp")
    experts = ctx_size * tp_size
    slots_rep = saved_pre.shape[2]
    capacity = slots_rep // experts
    hidden = saved_pre.shape[3] // 2
    half = model_width // n_dp
    devices = experts * n_dp
    slots_all = n_dp * slots_rep
    lanes = 512
    rows_per_chunk = capacity * half // lanes
    f32 = jnp.float32
    bf16 = jnp.bfloat16

    flat_routes = routes.reshape(-1)
    route_count = flat_routes.shape[0]
    idx = jnp.arange(route_count, dtype=jnp.int32)
    same = (flat_routes[:, None] == flat_routes[None, :]) & (idx[None, :] < idx[:, None])
    position = jnp.sum(same.astype(jnp.int32), axis=1)
    in_window = flat_routes < experts
    slot_index = jnp.where(in_window, flat_routes * capacity + position, -1)
    slot_ids = jnp.arange(experts * capacity, dtype=jnp.int32)
    route_hit = slot_index[:, None] == slot_ids[None, :]
    flat_probs = gate_probs.reshape(-1).astype(f32)

    blocks = half // lanes
    wide_rows = experts * capacity * blocks
    route_token = (idx // top_k).reshape(-1, 1)
    slot_filled = jnp.any(route_hit, axis=0)
    slot_token = jnp.where(slot_filled, jnp.sum(jnp.where(route_hit, route_token, 0), axis=0), -1)
    slot_prob = jnp.sum(jnp.where(route_hit, flat_probs[:, None], 0.0), axis=0)
    block_ids = jnp.arange(blocks, dtype=jnp.int32)
    row_key = jnp.where(
        slot_filled[:, None], block_ids[None, :] * tok_count + slot_token[:, None], -1
    ).reshape(wide_rows)
    row_prob = jnp.broadcast_to(slot_prob[:, None], (experts * capacity, blocks)).reshape(wide_rows)
    col_ids = jnp.arange(tok_count * blocks, dtype=jnp.int32)
    wide_hit = row_key[:, None] == col_ids[None, :]
    wide_select = wide_hit.astype(bf16)
    wide_prob_select = jnp.where(wide_hit, row_prob[:, None], 0.0).astype(bf16)
    gather_key = col_ids.reshape(blocks, tok_count, 1)
    gather_back = (gather_key == row_key.reshape(1, 1, -1)).astype(bf16)

    def dispatch(x, sel):
        xb = x.reshape(tok_count, n_dp * blocks, lanes).transpose(1, 0, 2)
        xb = xb.reshape(n_dp, blocks * tok_count, lanes)
        sent = jnp.einsum("qk,hkl->hql", sel, xb, preferred_element_type=f32).astype(bf16)
        got = lax.all_to_all(
            sent.reshape(devices, rows_per_chunk, lanes), WIRE, 0, 0, tiled=True
        )
        return got.reshape(slots_all, half)

    recv_pgrads = dispatch(out_grad, wide_prob_select)
    recv_rows = dispatch(activations, wide_select)

    own_saved = saved_pre[0, 0]
    if n_dp == 2:
        other_saved = lax.ppermute(own_saved, "dp", [(0, 1), (1, 0)])
        first = lax.axis_index("dp") == 0
        saved_rows = jnp.where(
            first,
            jnp.concatenate([own_saved, other_saved], axis=0),
            jnp.concatenate([other_saved, own_saved], axis=0),
        )
    else:
        saved_rows = lax.all_gather(own_saved, "dp", axis=0, tiled=True)
    weights = expert_weights[0]
    down_part = weights[:, 2 * hidden :]
    gate_up_part = weights[:, : 2 * hidden]

    partial_down = jnp.dot(recv_pgrads, down_part, preferred_element_type=f32)
    other_down = lax.ppermute(
        partial_down.astype(bf16), "dp", [(i, (i + 1) % n_dp) for i in range(n_dp)]
    )
    scaled_grad = partial_down + other_down.astype(f32)

    pre_gate = saved_rows[:, :hidden].astype(f32)
    pre_up = saved_rows[:, hidden:].astype(f32)
    sigmoid_gate = jax.nn.sigmoid(pre_gate)
    activated = pre_gate * sigmoid_gate
    hidden_act = activated * pre_up
    gate_factor = pre_up * sigmoid_gate * (1.0 + pre_gate * (1.0 - sigmoid_gate))
    activated, hidden_act, gate_factor = lax.optimization_barrier(
        (activated, hidden_act, gate_factor)
    )
    scaled_slot_prob = jnp.sum(hidden_act * scaled_grad, axis=1)
    gate_up_grad = jnp.concatenate(
        [scaled_grad * gate_factor, scaled_grad * activated], axis=1
    ).astype(bf16)

    row_grad = lax.dot_general(
        gate_up_grad, gate_up_part, (((1,), (1,)), ((), ())), preferred_element_type=f32
    ).astype(bf16)
    gate_up_term = lax.dot_general(
        recv_rows, gate_up_grad, (((0,), (0,)), ((), ())), preferred_element_type=f32
    )
    down_term = lax.dot_general(
        recv_pgrads, hidden_act.astype(bf16), (((0,), (0,)), ((), ())), preferred_element_type=f32
    )
    weight_grad = jnp.concatenate([gate_up_term, down_term], axis=1).astype(bf16)[None]

    back = lax.all_to_all(row_grad.reshape(devices, rows_per_chunk, lanes), WIRE, 0, 0, tiled=True)
    back = back.reshape(n_dp, -1, lanes)
    input_grad = jnp.einsum("ctk,hkl->thcl", gather_back, back, preferred_element_type=f32)
    input_grad = input_grad.reshape(tok_count, model_width).astype(bf16)

    back_probs = lax.all_to_all(scaled_slot_prob.reshape(devices, capacity), WIRE, 0, 0, tiled=True)
    back_probs = back_probs.reshape(n_dp, experts * capacity)[0]
    picked = jnp.sum(jnp.where(route_hit, back_probs[None, :], 0.0), axis=1)
    prob_grad = jnp.where(in_window, picked / flat_probs, 0.0)
    prob_grad = prob_grad.astype(bf16).reshape(tok_count, top_k)
    return (input_grad, prob_grad, weight_grad)


def solution(mesh):
    placed = (
        P(ALL, None),
        P(ALL, None),
        P(ALL, None),
        P(ALL, None),
        P(("ctx", "tp"), "dp", None, None),
        P(("ctx", "tp"), "dp", None),
    )
    return jax.shard_map(
        body,
        mesh=mesh,
        in_specs=placed,
        out_specs=(
            P(ALL, None),
            P(ALL, None),
            P(("ctx", "tp"), "dp", None),
        ),
        check_vma=False,
    )
```
